256 devices in a mesh: dp: 16 (over y, x_lo, core), ctx: 8 (over z), tp: 2 (over x_hi).
Axes of the slice: x: 4 (x_hi: 2, x_lo: 2; x = x_hi * 2 + x_lo), y: 4, z: 8, core: 2. Of those that a mesh axis runs over, the one named last changes fastest.
Arguments:
- tokens: bfloat16 [16, 2048, 8192], P('dp', 'ctx', 'tp'), may hold values from -6 to 6
- queries: bfloat16 [16, 2048, 8192], P('dp', 'ctx', 'tp'), may hold values from -180 to 180
- k_weight: bfloat16 [8192, 512], P('dp', 'tp'), may hold values from -0.0625 to 0.0625
- v_weight: bfloat16 [8192, 512], P('dp', 'tp'), may hold values from -0.0625 to 0.0625
- doc_blocks: int32 [16, 16], P('dp', 'ctx'), may hold values from 0 to 3, never falling along the last dimension, each value on 1 to 8 neighbouring positions
Outputs:
- context: bfloat16 [16, 2048, 8192], P('dp', 'ctx', 'tp')
The draws below stay inside these ranges and needn't reach their ends.
Inputs may be any that keep to these rules, and one draw needn't show every extreme that they name: `doc_blocks`: along each sequence the document numbers never fall; each document covers 1 to 8 whole blocks, one exactly 8.
All inputs are finite; a program needn't handle non-finite values.
Results may differ from the reference program's by a relative error of at most 0.012.
The reference program's roundings to bfloat16 on the way count: a program that leaves them out, or rounds other values in their place, can miss the bound.
Values may be sent and summed in bfloat16 or wider, within the bound.
No kernel may reach another device: no remote copies, remote signals or barrier semaphores. Data moves between devices by JAX's collectives and lax.ppermute only.
A program may use at most 192 MiB of HBM per device.

```python
import math
import jax
import jax.numpy as jnp
import numpy as np
from jax import lax

D = 8192
QH = 64
KVH = 4
HD = 128
BLOCK = 128
DOCS = 4
TOK_DEV = 256
SEQS = 16
LEN = 2048
NBLK = 16
N_CTX = 8


def draw_queries(key, part):
    key_base = jax.random.fold_in(key, 11)
    drawn = jnp.clip(jax.random.normal(key_base, (SEQS, LEN, QH * HD), jnp.float32), -4.0, 4.0)
    return drawn.astype(jnp.bfloat16)


def steps_of(rng, extent, pieces, low, high):
    level = 1.0
    for position, blocks in pieces:
        steps = jax.random.uniform(jax.random.fold_in(jax.random.fold_in(rng, 6), position), (blocks,), jnp.float32, low / len(pieces), high / len(pieces))
        level = level * jnp.repeat(jnp.exp(steps), extent[position] // blocks).reshape((-1,) + (1,) * (len(extent) - 1 - position))
    return level


def profile(amount, total, limit, skew):
    loads = [(1 << 20) // math.isqrt(standing ** skew) + 1 for standing in range(2, amount + 1)]
    spare, counts = total - limit - (amount - 1), [1] * (amount - 1)
    while spare > 0:
        candidates = [i for i in range(amount - 1) if counts[i] < limit]
        whole, left = sum([loads[i] for i in candidates]), spare
        for i in candidates:
            extra = min(limit - counts[i], max(1, left * loads[i] // whole), spare)
            counts[i] = counts[i] + extra
            spare = spare - extra
    return np.array([limit] + counts)


def ragged_sizes(key, count, total, most, lean):
    if count == 2:
        one = jax.random.randint(key, (), max(1, total - most), min(most, total - 1) + 1)
        return jnp.stack([one, total - one])
    tallies = jnp.asarray(profile(count, total, most, lean), jnp.int32)
    pairs = (count - 1) // 2
    donor, receiver = tallies[1:1 + 2 * pairs:2], tallies[2:2 + 2 * pairs:2]
    margin = jnp.minimum(donor - 1, most - receiver)
    moved = jax.random.randint(jax.random.fold_in(key, 1), (pairs,), 0, 1 << 20) % (margin + 1)
    tallies = tallies.at[1:1 + 2 * pairs:2].set(donor - moved).at[2:2 + 2 * pairs:2].set(receiver + moved)
    return tallies[jax.random.permutation(jax.random.fold_in(key, 2), count)]


def centred(own_key, extent, deviation, most, split=(), kind=jnp.bfloat16):
    level = steps_of(own_key, extent, split, -0.22, 0.18) if split else 1.0
    result = jax.random.normal(own_key, extent, jnp.float32) * deviation * level
    return jnp.minimum(jnp.maximum(result, -most), most).astype(kind)


def setup_inputs(seed: int = 0) -> dict:
    keys = jax.random.split(jax.random.key(seed), 6)
    return {
        "tokens": centred(keys[0], (SEQS, LEN, D), 1.0, 6.0, ((0, 16), (1, 8), (2, 2))),
        "queries": draw_queries(jax.random.fold_in(keys[5], 71), 0),
        "k_weight": centred(keys[2], (D, KVH * HD), D ** -0.5, 0.0625, ((0, 16), (1, 2))),
        "v_weight": centred(keys[3], (D, KVH * HD), D ** -0.5, 0.0625, ((0, 16), (1, 2))),
        "doc_blocks": jax.vmap(lambda own: jnp.searchsorted(jnp.cumsum(ragged_sizes(own, DOCS, NBLK, NBLK // 2, 0)), jnp.arange(NBLK), side="right"))(jax.random.split(keys[4], SEQS)).reshape((SEQS, NBLK)).astype(jnp.int32),
    }


ROPE_BASE = 500000.0
YARN_FACTOR = 16.0
PRETRAIN_CONTEXT = 8192.0
BETA_FAST = 32.0
BETA_SLOW = 1.0
ATTN_FACTOR = (1.0 + 0.1 * math.log(16.0)) ** 2

def yarn_tables(positions):
    counter = jnp.arange(HD // 2, dtype=jnp.float32)
    base_freq = ROPE_BASE ** (-2.0 * counter / HD)
    wave_ratio = PRETRAIN_CONTEXT * base_freq / (2.0 * math.pi)
    ramp_value = jnp.clip((wave_ratio - BETA_SLOW) / (BETA_FAST - BETA_SLOW), 0.0, 1.0)
    frequency = ramp_value * base_freq + (1.0 - ramp_value) * base_freq / YARN_FACTOR
    angles = positions.astype(jnp.float32)[:, None] * frequency[None, :]
    cosine = jnp.cos(angles)
    sine_table = jnp.sin(angles)
    return (jnp.concatenate([cosine, cosine], axis=-1), jnp.concatenate([sine_table, sine_table], axis=-1))

def rotate(vectors, cosine, sine_table):
    half_width = vectors.shape[-1] // 2
    lower_half = vectors[..., :half_width]
    upper_half = vectors[..., half_width:]
    turned = jnp.concatenate([-upper_half, lower_half], axis=-1)
    return vectors * cosine[:, None, :] + turned * sine_table[:, None, :]

def reference(tokens, queries, k_weight, v_weight, doc_blocks):
    group_size = QH // KVH

    def one_sequence(packed):
        seq_tokens, seq_queries, seq_docs = packed
        key_proj = jnp.dot(seq_tokens, k_weight, preferred_element_type=jnp.float32)
        value_proj = jnp.dot(seq_tokens, v_weight, preferred_element_type=jnp.float32)
        positions = jnp.arange(LEN, dtype=jnp.int32)
        cosine, sine_table = yarn_tables(positions)
        key_rows = rotate(key_proj.reshape(LEN, KVH, HD), cosine, sine_table).astype(jnp.bfloat16)
        value_rows = value_proj.reshape(LEN, KVH, HD).astype(jnp.bfloat16)
        query_rot = (rotate(seq_queries.astype(jnp.float32).reshape(LEN, QH, HD), cosine, sine_table) * (ATTN_FACTOR / math.sqrt(HD))).astype(jnp.bfloat16)
        token_docs = jnp.repeat(seq_docs, BLOCK)
        key_float = key_rows.astype(jnp.float32)
        value_float = value_rows.astype(jnp.float32)

        def one_block(block_id):
            begin_row = (block_id * TOK_DEV).astype(jnp.int32)
            query_block = lax.dynamic_slice_in_dim(query_rot, begin_row, TOK_DEV, 0).astype(jnp.float32)
            query_block = query_block.reshape(TOK_DEV, KVH, group_size, HD)
            query_pos = begin_row + jnp.arange(TOK_DEV, dtype=jnp.int32)
            query_docs = lax.dynamic_slice_in_dim(token_docs, begin_row, TOK_DEV, 0)
            visible = (positions[None, :] <= query_pos[:, None]) & (token_docs[None, :] == query_docs[:, None])
            scores = jnp.einsum('qkgd,nkd->kgqn', query_block, key_float)
            scores = jnp.where(visible, scores, -jnp.inf)
            row_top = lax.optimization_barrier(jnp.max(scores, axis=-1, keepdims=True))
            weights = jnp.exp(scores - row_top)
            denominator = lax.optimization_barrier(jnp.sum(weights, axis=-1))
            mixed_values = jnp.einsum('kgqn,nkd->kgqd', weights.astype(jnp.bfloat16).astype(jnp.float32), value_float)
            attended = mixed_values / denominator[..., None]
            return attended.transpose(2, 0, 1, 3).reshape(TOK_DEV, QH * HD).astype(jnp.bfloat16)
        blocks = lax.map(one_block, jnp.arange(N_CTX, dtype=jnp.int32))
        return blocks.reshape(LEN, QH * HD)
    return lax.map(one_sequence, (tokens, queries, doc_blocks))
```

```python
import math

import jax
import jax.numpy as jnp
from jax import lax
from jax.sharding import PartitionSpec as P

HD = 128
BLOCK = 128
LOOKBACK = 7


ROPE_BASE = 500000.0
YARN_FACTOR = 16.0
PRETRAIN_CONTEXT = 8192.0
BETA_FAST = 32.0
BETA_SLOW = 1.0
ATTN_FACTOR = (1.0 + 0.1 * math.log(16.0)) ** 2
MASKED_SCORE = -1e30


def yarn_tables(positions):
    counter = jnp.arange(HD // 2, dtype=jnp.float32)
    base_freq = ROPE_BASE ** (-2.0 * counter / HD)
    wave_ratio = PRETRAIN_CONTEXT * base_freq / (2.0 * math.pi)
    ramp_value = jnp.clip((wave_ratio - BETA_SLOW) / (BETA_FAST - BETA_SLOW), 0.0, 1.0)
    frequency = ramp_value * base_freq + (1.0 - ramp_value) * base_freq / YARN_FACTOR
    angles = positions.astype(jnp.float32)[:, None] * frequency[None, :]
    cosine = jnp.cos(angles)
    sine_table = jnp.sin(angles)
    return (
        jnp.concatenate([cosine, cosine], axis=-1),
        jnp.concatenate([sine_table, sine_table], axis=-1),
    )


def rotate(vectors, cosine, sine_table):
    half_width = vectors.shape[-1] // 2
    lower_half = vectors[..., :half_width]
    upper_half = vectors[..., half_width:]
    turned = jnp.concatenate([-upper_half, lower_half], axis=-1)
    return vectors * cosine[:, None, :] + turned * sine_table[:, None, :]


def shift_pairs(count, step):
    return [(i, i + step) for i in range(count - step)]


def make_body(n_ctx):
    def body(tokens, queries, k_weight, v_weight, doc_blocks):
        local_tokens = tokens[0]
        row_count, feat_half = local_tokens.shape
        ctx_rank = lax.axis_index("ctx")
        tp_rank = lax.axis_index("tp")
        kv_width = k_weight.shape[1]
        kv_heads = kv_width // HD

        joined = jnp.concatenate([k_weight, v_weight], axis=1)
        weights = lax.all_gather(joined, "dp", axis=0, tiled=True)
        weights = weights.reshape(2, feat_half, 2 * kv_width)
        partner_tokens = lax.ppermute(local_tokens, "tp", [(0, 1), (1, 0)])
        proj = jnp.dot(local_tokens, weights[tp_rank], preferred_element_type=jnp.float32)
        proj = proj + jnp.dot(
            partner_tokens, weights[1 - tp_rank], preferred_element_type=jnp.float32
        )

        positions = ctx_rank * row_count + jnp.arange(row_count, dtype=jnp.int32)
        cosine, sine_table = yarn_tables(positions)
        key_rows = (
            rotate(proj[:, :kv_width].reshape(row_count, kv_heads, HD), cosine, sine_table)
            .reshape(row_count, kv_width)
            .astype(jnp.bfloat16)
        )
        value_rows = proj[:, kv_width:].astype(jnp.bfloat16)
        kv_rows = jnp.concatenate([key_rows, value_rows], axis=1)

        local_docs = doc_blocks[0]
        blocks_here = row_count // BLOCK
        window_kv = []
        window_docs = []
        need = LOOKBACK
        step = 1
        while need > 0:
            take = min(need, blocks_here)
            pairs = shift_pairs(n_ctx, step)
            window_kv.insert(0, lax.ppermute(kv_rows[(blocks_here - take) * BLOCK:], "ctx", pairs))
            window_docs.insert(0, lax.ppermute(local_docs[blocks_here - take:], "ctx", pairs))
            need -= take
            step += 1
        window_kv.append(kv_rows)
        window_docs.append(local_docs)
        kv_all = jnp.concatenate(window_kv, axis=0)
        key_docs = jnp.repeat(jnp.concatenate(window_docs, axis=0), BLOCK)
        height = kv_all.shape[0]
        key_pos = ctx_rank * row_count - (height - row_count) + jnp.arange(height, dtype=jnp.int32)

        local_queries = queries[0]
        query_heads = local_queries.shape[1] // HD
        group_size = query_heads // kv_heads
        query_rot = (
            (
                rotate(
                    local_queries.astype(jnp.float32).reshape(row_count, query_heads, HD),
                    cosine,
                    sine_table,
                )
                * (ATTN_FACTOR / math.sqrt(HD))
            )
            .astype(jnp.bfloat16)
            .reshape(row_count, kv_heads, group_size, HD)
        )
        query_docs = jnp.repeat(local_docs, BLOCK)
        visible = (
            (key_pos[None, :] <= positions[:, None])
            & (key_pos[None, :] >= 0)
            & (key_docs[None, :] == query_docs[:, None])
        )
        keys = kv_all[:, :kv_width].reshape(height, kv_heads, HD)
        values = kv_all[:, kv_width:].reshape(height, kv_heads, HD)
        scores = jnp.einsum("qkgd,nkd->kgqn", query_rot, keys, preferred_element_type=jnp.float32)
        scores = jnp.where(visible, scores, MASKED_SCORE)
        row_max = jnp.max(scores, axis=-1)
        probs = jnp.where(visible, jnp.exp(scores - row_max[..., None]), 0.0)
        row_sum = jnp.sum(probs, axis=-1)
        mixed = jnp.einsum(
            "kgqn,nkd->kgqd", probs.astype(jnp.bfloat16), values, preferred_element_type=jnp.float32
        )
        attended = mixed / row_sum[..., None]
        context = (
            attended.transpose(2, 0, 1, 3).reshape(row_count, query_heads * HD).astype(jnp.bfloat16)
        )
        return context[None]

    return body


def solution(mesh):
    placed = (
        P("dp", "ctx", "tp"),
        P("dp", "ctx", "tp"),
        P("dp", "tp"),
        P("dp", "tp"),
        P("dp", "ctx"),
    )
    return jax.shard_map(
        make_body(mesh.shape["ctx"]),
        mesh=mesh,
        in_specs=placed,
        out_specs=P("dp", "ctx", "tp"),
        check_vma=False,
    )
```

```python
import math

import jax
import jax.numpy as jnp
from jax import lax
from jax.experimental import pallas as pl
from jax.experimental.pallas import tpu as pltpu
from jax.sharding import PartitionSpec as P

HD = 128
BLOCK = 128
LOOKBACK = 7


ROPE_BASE = 500000.0
YARN_FACTOR = 16.0
PRETRAIN_CONTEXT = 8192.0
BETA_FAST = 32.0
BETA_SLOW = 1.0
ATTN_FACTOR = (1.0 + 0.1 * math.log(16.0)) ** 2
MASKED_SCORE = -1e30


def yarn_tables(positions):
    counter = jnp.arange(HD // 2, dtype=jnp.float32)
    base_freq = ROPE_BASE ** (-2.0 * counter / HD)
    wave_ratio = PRETRAIN_CONTEXT * base_freq / (2.0 * math.pi)
    ramp_value = jnp.clip((wave_ratio - BETA_SLOW) / (BETA_FAST - BETA_SLOW), 0.0, 1.0)
    frequency = ramp_value * base_freq + (1.0 - ramp_value) * base_freq / YARN_FACTOR
    angles = positions.astype(jnp.float32)[:, None] * frequency[None, :]
    cosine = jnp.cos(angles)
    sine_table = jnp.sin(angles)
    return (
        jnp.concatenate([cosine, cosine], axis=-1),
        jnp.concatenate([sine_table, sine_table], axis=-1),
    )


def rotate(vectors, cosine, sine_table):
    half_width = vectors.shape[-1] // 2
    lower_half = vectors[..., :half_width]
    upper_half = vectors[..., half_width:]
    turned = jnp.concatenate([-upper_half, lower_half], axis=-1)
    return vectors * cosine[:, None, :] + turned * sine_table[:, None, :]


def flash_kernel(lo_ref, q_ref, k_ref, v_ref, o_ref, qs_ref, m_ref, l_ref, acc_ref):
    qb = pl.program_id(0)
    rows = o_ref.shape[0]
    group = o_ref.shape[1] // HD
    for g in range(group):
        qs_ref[g * rows:(g + 1) * rows, :] = q_ref[:, g * HD:(g + 1) * HD]
    m_ref[...] = jnp.full(m_ref.shape, MASKED_SCORE, jnp.float32)
    l_ref[...] = jnp.zeros(l_ref.shape, jnp.float32)
    acc_ref[...] = jnp.zeros(acc_ref.shape, jnp.float32)
    own = LOOKBACK + qb
    col = lax.broadcasted_iota(jnp.int32, (group, rows, BLOCK), 2)
    row = lax.broadcasted_iota(jnp.int32, (group, rows, BLOCK), 1)

    def step(j, carry):
        start = pl.multiple_of(j * BLOCK, BLOCK)
        keys = k_ref[pl.ds(start, BLOCK), :]
        values = v_ref[pl.ds(start, BLOCK), :]
        scores = lax.dot_general(
            qs_ref[...], keys, (((1,), (1,)), ((), ())), preferred_element_type=jnp.float32
        )
        keep = col <= row + (own - j) * BLOCK
        scores = jnp.where(keep, scores.reshape(group, rows, BLOCK), MASKED_SCORE)
        scores = scores.reshape(group * rows, BLOCK)
        m_old = m_ref[...]
        m_new = jnp.maximum(m_old, jnp.max(scores, axis=1, keepdims=True))
        alpha = jnp.exp(m_old - m_new)
        probs = jnp.exp(scores - m_new)
        l_ref[...] = alpha * l_ref[...] + jnp.sum(probs, axis=1, keepdims=True)
        acc_ref[...] = alpha * acc_ref[...] + jnp.dot(
            probs.astype(jnp.bfloat16), values, preferred_element_type=jnp.float32
        )
        m_ref[...] = m_new
        return carry

    lax.fori_loop(lo_ref[qb], own + 1, step, 0)
    result = acc_ref[...] / l_ref[...]
    for g in range(group):
        o_ref[:, g * HD:(g + 1) * HD] = result[g * rows:(g + 1) * rows].astype(o_ref.dtype)


def flash_attention(lo, query_rot, kv_all, kv_heads):
    row_count, width = query_rot.shape
    height = kv_all.shape[0]
    q_blocks = row_count // BLOCK
    group_width = width // kv_heads
    group = group_width // HD
    grid_spec = pltpu.PrefetchScalarGridSpec(
        num_scalar_prefetch=1,
        grid=(q_blocks, kv_heads),
        in_specs=[
            pl.BlockSpec((BLOCK, group_width), lambda qb, h, lo: (qb, h)),
            pl.BlockSpec((height, HD), lambda qb, h, lo: (0, h)),
            pl.BlockSpec((height, HD), lambda qb, h, lo: (0, kv_heads + h)),
        ],
        out_specs=pl.BlockSpec((BLOCK, group_width), lambda qb, h, lo: (qb, h)),
        scratch_shapes=[
            pltpu.VMEM((group * BLOCK, HD), jnp.bfloat16),
            pltpu.VMEM((group * BLOCK, 1), jnp.float32),
            pltpu.VMEM((group * BLOCK, 1), jnp.float32),
            pltpu.VMEM((group * BLOCK, HD), jnp.float32),
        ],
    )
    visits = q_blocks * kv_heads * (LOOKBACK + 1) // 2
    return pl.pallas_call(
        flash_kernel,
        grid_spec=grid_spec,
        out_shape=jax.ShapeDtypeStruct((row_count, width), jnp.bfloat16),
        cost_estimate=pl.CostEstimate(
            flops=visits * 4 * group * BLOCK * BLOCK * HD,
            transcendentals=visits * group * BLOCK * BLOCK,
            bytes_accessed=4 * row_count * width + 2 * kv_all.size,
        ),
    )(lo, query_rot, kv_all, kv_all)


def shift_pairs(count, step):
    return [(i, i + step) for i in range(count - step)]


def make_body(n_ctx):
    def body(tokens, queries, k_weight, v_weight, doc_blocks):
        local_tokens = tokens[0]
        row_count, feat_half = local_tokens.shape
        ctx_rank = lax.axis_index("ctx")
        tp_rank = lax.axis_index("tp")
        kv_width = k_weight.shape[1]
        kv_heads = kv_width // HD

        joined = jnp.concatenate([k_weight, v_weight], axis=1)
        weights = lax.all_gather(joined, "dp", axis=0, tiled=True)
        weights = weights.reshape(2, feat_half, 2 * kv_width)
        partner_tokens = lax.ppermute(local_tokens, "tp", [(0, 1), (1, 0)])
        proj = jnp.dot(local_tokens, weights[tp_rank], preferred_element_type=jnp.float32)
        proj = proj + jnp.dot(
            partner_tokens, weights[1 - tp_rank], preferred_element_type=jnp.float32
        )

        positions = ctx_rank * row_count + jnp.arange(row_count, dtype=jnp.int32)
        cosine, sine_table = yarn_tables(positions)
        key_rows = (
            rotate(proj[:, :kv_width].reshape(row_count, kv_heads, HD), cosine, sine_table)
            .reshape(row_count, kv_width)
            .astype(jnp.bfloat16)
        )
        value_rows = proj[:, kv_width:].astype(jnp.bfloat16)
        kv_rows = jnp.concatenate([key_rows, value_rows], axis=1)

        local_docs = doc_blocks[0]
        blocks_here = row_count // BLOCK
        doc_rows = jnp.zeros((16, 2 * kv_width), jnp.bfloat16)
        window_kv = []
        window_docs = []
        need = LOOKBACK
        step = 1
        while need > 0:
            take = min(need, blocks_here)
            pairs = shift_pairs(n_ctx, step)
            tagged = doc_rows.at[0, :take].set(local_docs[blocks_here - take:].astype(jnp.bfloat16))
            payload = jnp.concatenate([kv_rows[(blocks_here - take) * BLOCK:], tagged], axis=0)
            arrived = lax.ppermute(payload, "ctx", pairs)
            window_kv.insert(0, arrived[:take * BLOCK])
            window_docs.insert(0, arrived[take * BLOCK, :take].astype(jnp.int32))
            need -= take
            step += 1
        window_kv.append(kv_rows)
        window_docs.append(local_docs)
        kv_all = jnp.concatenate(window_kv, axis=0)
        block_docs = jnp.concatenate(window_docs, axis=0)
        window_blocks = block_docs.shape[0]
        block_index = jnp.arange(window_blocks, dtype=jnp.int32)
        block_valid = ctx_rank * blocks_here - LOOKBACK + block_index >= 0
        own = LOOKBACK + jnp.arange(blocks_here, dtype=jnp.int32)
        same = (
            block_valid[None, :]
            & (block_docs[None, :] == local_docs[:, None])
            & (block_index[None, :] <= own[:, None])
        )
        lo = own + 1 - jnp.sum(same.astype(jnp.int32), axis=1)

        local_queries = queries[0]
        query_heads = local_queries.shape[1] // HD
        query_rot = (
            (
                rotate(
                    local_queries.astype(jnp.float32).reshape(row_count, query_heads, HD),
                    cosine,
                    sine_table,
                )
                * (ATTN_FACTOR / math.sqrt(HD))
            )
            .reshape(row_count, query_heads * HD)
            .astype(jnp.bfloat16)
        )
        context = flash_attention(lo, query_rot, kv_all, kv_heads)
        return context[None]

    return body


def solution(mesh):
    placed = (
        P("dp", "ctx", "tp"),
        P("dp", "ctx", "tp"),
        P("dp", "tp"),
        P("dp", "tp"),
        P("dp", "ctx"),
    )
    return jax.shard_map(
        make_body(mesh.shape["ctx"]),
        mesh=mesh,
        in_specs=placed,
        out_specs=P("dp", "ctx", "tp"),
        check_vma=False,
    )
```

```python
import math

import jax
import jax.numpy as jnp
from jax import lax
from jax.experimental import pallas as pl
from jax.experimental.pallas import tpu as pltpu
from jax.sharding import PartitionSpec as P

HD = 128
BLOCK = 128
LOOKBACK = 7


ROPE_BASE = 500000.0
YARN_FACTOR = 16.0
PRETRAIN_CONTEXT = 8192.0
BETA_FAST = 32.0
BETA_SLOW = 1.0
ATTN_FACTOR = (1.0 + 0.1 * math.log(16.0)) ** 2
MASKED_SCORE = -1e30


def yarn_tables(positions):
    counter = jnp.arange(HD // 2, dtype=jnp.float32)
    base_freq = ROPE_BASE ** (-2.0 * counter / HD)
    wave_ratio = PRETRAIN_CONTEXT * base_freq / (2.0 * math.pi)
    ramp_value = jnp.clip((wave_ratio - BETA_SLOW) / (BETA_FAST - BETA_SLOW), 0.0, 1.0)
    frequency = ramp_value * base_freq + (1.0 - ramp_value) * base_freq / YARN_FACTOR
    angles = positions.astype(jnp.float32)[:, None] * frequency[None, :]
    cosine = jnp.cos(angles)
    sine_table = jnp.sin(angles)
    return (
        jnp.concatenate([cosine, cosine], axis=-1),
        jnp.concatenate([sine_table, sine_table], axis=-1),
    )


def rotate(vectors, cosine, sine_table):
    half_width = vectors.shape[-1] // 2
    lower_half = vectors[..., :half_width]
    upper_half = vectors[..., half_width:]
    turned = jnp.concatenate([-upper_half, lower_half], axis=-1)
    return vectors * cosine[:, None, :] + turned * sine_table[:, None, :]


def dense_kernel(vis_ref, q_ref, k_ref, v_ref, o_ref, qs_ref):
    rows = o_ref.shape[0]
    group = o_ref.shape[1] // HD
    for g in range(group):
        qs_ref[g * rows:(g + 1) * rows, :] = q_ref[:, g * HD:(g + 1) * HD]
    visible = vis_ref[...] != 0
    keys = k_ref[...]
    values = v_ref[...]
    height = keys.shape[0]
    part = group // 2
    for half in range(2):
        stacked = qs_ref[half * part * rows:(half + 1) * part * rows, :]
        scores = lax.dot_general(
            stacked, keys, (((1,), (1,)), ((), ())), preferred_element_type=jnp.float32
        )
        scores = jnp.where(visible[None], scores.reshape(part, rows, height), MASKED_SCORE)
        row_max = jnp.max(scores, axis=2, keepdims=True)
        probs = jnp.where(visible[None], jnp.exp(scores - row_max), 0.0)
        row_sum = jnp.sum(probs, axis=2, keepdims=True)
        mixed = jnp.dot(
            probs.reshape(part * rows, height).astype(jnp.bfloat16),
            values,
            preferred_element_type=jnp.float32,
        )
        result = mixed.reshape(part, rows, HD) / row_sum
        for g in range(part):
            head = half * part + g
            o_ref[:, head * HD:(head + 1) * HD] = result[g].astype(o_ref.dtype)


def dense_attention(visible, query_rot, kv_all, kv_heads):
    row_count, width = query_rot.shape
    height = kv_all.shape[0]
    q_blocks = row_count // BLOCK
    group_width = width // kv_heads
    group = group_width // HD
    return pl.pallas_call(
        dense_kernel,
        grid=(q_blocks, kv_heads),
        in_specs=[
            pl.BlockSpec((BLOCK, height), lambda qb, h: (qb, 0)),
            pl.BlockSpec((BLOCK, group_width), lambda qb, h: (qb, h)),
            pl.BlockSpec((height, HD), lambda qb, h: (0, h)),
            pl.BlockSpec((height, HD), lambda qb, h: (0, kv_heads + h)),
        ],
        out_specs=pl.BlockSpec((BLOCK, group_width), lambda qb, h: (qb, h)),
        scratch_shapes=[pltpu.VMEM((group * BLOCK, HD), jnp.bfloat16)],
        out_shape=jax.ShapeDtypeStruct((row_count, width), jnp.bfloat16),
        compiler_params=pltpu.CompilerParams(vmem_limit_bytes=48 * 1024 * 1024),
        cost_estimate=pl.CostEstimate(
            flops=4 * row_count * width * height,
            transcendentals=row_count * (width // HD) * height,
            bytes_accessed=4 * row_count * width + 2 * kv_all.size + 4 * row_count * height,
        ),
    )(visible, query_rot, kv_all, kv_all)


def shift_pairs(count, step):
    return [(i, i + step) for i in range(count - step)]


def make_body(n_ctx):
    def body(tokens, queries, k_weight, v_weight, doc_blocks):
        local_tokens = tokens[0]
        row_count, feat_half = local_tokens.shape
        ctx_rank = lax.axis_index("ctx")
        tp_rank = lax.axis_index("tp")
        kv_width = k_weight.shape[1]
        kv_heads = kv_width // HD

        joined = jnp.concatenate([k_weight, v_weight], axis=1)
        weights = lax.all_gather(joined, "dp", axis=0, tiled=True)
        weights = weights.reshape(2, feat_half, 2 * kv_width)
        partner_tokens = lax.ppermute(local_tokens, "tp", [(0, 1), (1, 0)])
        proj = jnp.dot(local_tokens, weights[tp_rank], preferred_element_type=jnp.float32)
        proj = proj + jnp.dot(
            partner_tokens, weights[1 - tp_rank], preferred_element_type=jnp.float32
        )

        positions = ctx_rank * row_count + jnp.arange(row_count, dtype=jnp.int32)
        cosine, sine_table = yarn_tables(positions)
        key_rows = (
            rotate(proj[:, :kv_width].reshape(row_count, kv_heads, HD), cosine, sine_table)
            .reshape(row_count, kv_width)
            .astype(jnp.bfloat16)
        )
        value_rows = proj[:, kv_width:].astype(jnp.bfloat16)
        kv_rows = jnp.concatenate([key_rows, value_rows], axis=1)

        local_docs = doc_blocks[0]
        blocks_here = row_count // BLOCK
        doc_rows = jnp.zeros((16, 2 * kv_width), jnp.bfloat16)
        window_kv = []
        window_docs = []
        need = LOOKBACK
        step = 1
        while need > 0:
            take = min(need, blocks_here)
            pairs = shift_pairs(n_ctx, step)
            tagged = doc_rows.at[0, :take].set(local_docs[blocks_here - take:].astype(jnp.bfloat16))
            payload = jnp.concatenate([kv_rows[(blocks_here - take) * BLOCK:], tagged], axis=0)
            arrived = lax.ppermute(payload, "ctx", pairs)
            window_kv.insert(0, arrived[:take * BLOCK])
            window_docs.insert(0, arrived[take * BLOCK, :take].astype(jnp.int32))
            need -= take
            step += 1
        window_kv.append(kv_rows)
        window_docs.append(local_docs)
        kv_all = jnp.concatenate(window_kv, axis=0)
        block_docs = jnp.concatenate(window_docs, axis=0)
        height = kv_all.shape[0]
        key_pos = ctx_rank * row_count - (height - row_count) + jnp.arange(height, dtype=jnp.int32)
        key_docs = jnp.repeat(block_docs, BLOCK)
        query_docs = jnp.repeat(local_docs, BLOCK)
        visible = (
            (key_pos[None, :] <= positions[:, None])
            & (key_pos[None, :] >= 0)
            & (key_docs[None, :] == query_docs[:, None])
        ).astype(jnp.int32)

        local_queries = queries[0]
        query_heads = local_queries.shape[1] // HD
        query_rot = (
            (
                rotate(
                    local_queries.astype(jnp.float32).reshape(row_count, query_heads, HD),
                    cosine,
                    sine_table,
                )
                * (ATTN_FACTOR / math.sqrt(HD))
            )
            .reshape(row_count, query_heads * HD)
            .astype(jnp.bfloat16)
        )
        context = dense_attention(visible, query_rot, kv_all, kv_heads)
        return context[None]

    return body


def solution(mesh):
    placed = (
        P("dp", "ctx", "tp"),
        P("dp", "ctx", "tp"),
        P("dp", "tp"),
        P("dp", "tp"),
        P("dp", "ctx"),
    )
    return jax.shard_map(
        make_body(mesh.shape["ctx"]),
        mesh=mesh,
        in_specs=placed,
        out_specs=P("dp", "ctx", "tp"),
        check_vma=False,
    )
```

```python
import math

import jax
import jax.numpy as jnp
from jax import lax
from jax.experimental import pallas as pl
from jax.experimental.pallas import tpu as pltpu
from jax.sharding import PartitionSpec as P

HD = 128
BLOCK = 128
LOOKBACK = 7


ROPE_BASE = 500000.0
YARN_FACTOR = 16.0
PRETRAIN_CONTEXT = 8192.0
BETA_FAST = 32.0
BETA_SLOW = 1.0
ATTN_FACTOR = (1.0 + 0.1 * math.log(16.0)) ** 2
MASKED_SCORE = -1e30


def yarn_tables(positions):
    counter = jnp.arange(HD // 2, dtype=jnp.float32)
    base_freq = ROPE_BASE ** (-2.0 * counter / HD)
    wave_ratio = PRETRAIN_CONTEXT * base_freq / (2.0 * math.pi)
    ramp_value = jnp.clip((wave_ratio - BETA_SLOW) / (BETA_FAST - BETA_SLOW), 0.0, 1.0)
    frequency = ramp_value * base_freq + (1.0 - ramp_value) * base_freq / YARN_FACTOR
    angles = positions.astype(jnp.float32)[:, None] * frequency[None, :]
    cosine = jnp.cos(angles)
    sine_table = jnp.sin(angles)
    return (
        jnp.concatenate([cosine, cosine], axis=-1),
        jnp.concatenate([sine_table, sine_table], axis=-1),
    )


def rotate(vectors, cosine, sine_table):
    half_width = vectors.shape[-1] // 2
    lower_half = vectors[..., :half_width]
    upper_half = vectors[..., half_width:]
    turned = jnp.concatenate([-upper_half, lower_half], axis=-1)
    return vectors * cosine[:, None, :] + turned * sine_table[:, None, :]


def dense_kernel(vis_ref, q_ref, k_ref, v_ref, o_ref, qs_ref):
    rows = o_ref.shape[0]
    group = o_ref.shape[1] // HD
    for g in range(group):
        qs_ref[g * rows:(g + 1) * rows, :] = q_ref[:, g * HD:(g + 1) * HD]
    visible = vis_ref[...] != 0
    keys = k_ref[...]
    values = v_ref[...]
    height = keys.shape[0]
    part = group // 2
    for half in range(2):
        stacked = qs_ref[half * part * rows:(half + 1) * part * rows, :]
        scores = lax.dot_general(
            stacked, keys, (((1,), (1,)), ((), ())), preferred_element_type=jnp.float32
        )
        scores = jnp.where(visible[None], scores.reshape(part, rows, height), MASKED_SCORE)
        row_max = jnp.max(scores, axis=2, keepdims=True)
        probs = jnp.where(visible[None], jnp.exp(scores - row_max), 0.0)
        row_sum = jnp.sum(probs, axis=2, keepdims=True)
        mixed = jnp.dot(
            probs.reshape(part * rows, height).astype(jnp.bfloat16),
            values,
            preferred_element_type=jnp.float32,
        )
        result = mixed.reshape(part, rows, HD) / row_sum
        for g in range(part):
            head = half * part + g
            o_ref[:, head * HD:(head + 1) * HD] = result[g].astype(o_ref.dtype)


def dense_attention(visible, query_rot, kv_all, kv_heads):
    row_count, width = query_rot.shape
    height = kv_all.shape[0]
    q_blocks = row_count // BLOCK
    group_width = width // kv_heads
    group = group_width // HD
    return pl.pallas_call(
        dense_kernel,
        grid=(q_blocks, kv_heads),
        in_specs=[
            pl.BlockSpec((BLOCK, height), lambda qb, h: (qb, 0)),
            pl.BlockSpec((BLOCK, group_width), lambda qb, h: (qb, h)),
            pl.BlockSpec((height, HD), lambda qb, h: (0, h)),
            pl.BlockSpec((height, HD), lambda qb, h: (0, kv_heads + h)),
        ],
        out_specs=pl.BlockSpec((BLOCK, group_width), lambda qb, h: (qb, h)),
        scratch_shapes=[pltpu.VMEM((group * BLOCK, HD), jnp.bfloat16)],
        out_shape=jax.ShapeDtypeStruct((row_count, width), jnp.bfloat16),
        compiler_params=pltpu.CompilerParams(vmem_limit_bytes=48 * 1024 * 1024),
        cost_estimate=pl.CostEstimate(
            flops=4 * row_count * width * height,
            transcendentals=row_count * (width // HD) * height,
            bytes_accessed=4 * row_count * width + 2 * kv_all.size + 4 * row_count * height,
        ),
    )(visible, query_rot, kv_all, kv_all)


def shift_pairs(count, step):
    return [(i, i + step) for i in range(count - step)]


def x_shift_pairs(n_dpc, n_tp, direction):
    pairs = []
    for dpc in range(n_dpc):
        for tp in range(n_tp):
            x = 2 * tp + dpc % 2
            moved = (x + direction) % (2 * n_tp)
            target = (dpc - dpc % 2 + moved % 2) * n_tp + moved // 2
            pairs.append((dpc * n_tp + tp, target))
    return pairs


def make_body(n_dpc, n_ctx, n_tp):
    def body(tokens, queries, k_weight, v_weight, doc_blocks):
        local_tokens = tokens[0]
        row_count, feat_half = local_tokens.shape
        ctx_rank = lax.axis_index("ctx")
        tp_rank = lax.axis_index("tp")
        core_rank = lax.axis_index("core")
        kv_width = k_weight.shape[1]
        kv_heads = kv_width // HD
        rows_per_block = k_weight.shape[0]

        half_rows = row_count // 2
        forward = x_shift_pairs(n_dpc, n_tp, 1)
        backward = x_shift_pairs(n_dpc, n_tp, -1)
        via_next = lax.ppermute(local_tokens[:half_rows], ("dpc", "tp"), forward)
        via_prev = lax.ppermute(local_tokens[half_rows:], ("dpc", "tp"), backward)
        via_next = lax.ppermute(via_next, ("dpc", "tp"), forward)
        via_prev = lax.ppermute(via_prev, ("dpc", "tp"), backward)
        partner_tokens = jnp.concatenate([via_next, via_prev], axis=0)

        joined = jnp.concatenate([k_weight, v_weight], axis=1)
        mine = lax.all_gather(joined, "dpc", axis=0, tiled=False)
        other = lax.ppermute(mine, "core", [(0, 1), (1, 0)])
        per_half = n_dpc // n_tp

        def part(chunk, source_tp, weights, parity):
            chunk = chunk.reshape(row_count, per_half, 2, rows_per_block)
            chunk = lax.dynamic_index_in_dim(chunk, parity, axis=2, keepdims=False)
            rows = lax.dynamic_slice_in_dim(weights, source_tp * per_half, per_half, 0)
            return jnp.einsum("qjf,jfn->qn", chunk, rows, preferred_element_type=jnp.float32)

        proj = part(local_tokens, tp_rank, mine, core_rank)
        proj = proj + part(local_tokens, tp_rank, other, 1 - core_rank)
        proj = proj + part(partner_tokens, 1 - tp_rank, mine, core_rank)
        proj = proj + part(partner_tokens, 1 - tp_rank, other, 1 - core_rank)

        positions = ctx_rank * row_count + jnp.arange(row_count, dtype=jnp.int32)
        cosine, sine_table = yarn_tables(positions)
        key_rows = (
            rotate(proj[:, :kv_width].reshape(row_count, kv_heads, HD), cosine, sine_table)
            .reshape(row_count, kv_width)
            .astype(jnp.bfloat16)
        )
        value_rows = proj[:, kv_width:].astype(jnp.bfloat16)
        kv_rows = jnp.concatenate([key_rows, value_rows], axis=1)

        local_docs = doc_blocks[0]
        blocks_here = row_count // BLOCK
        doc_rows = jnp.zeros((16, 2 * kv_width), jnp.bfloat16)
        window_kv = []
        window_docs = []
        need = LOOKBACK
        step = 1
        while need > 0:
            take = min(need, blocks_here)
            pairs = shift_pairs(n_ctx, step)
            tagged = doc_rows.at[0, :take].set(local_docs[blocks_here - take:].astype(jnp.bfloat16))
            payload = jnp.concatenate([kv_rows[(blocks_here - take) * BLOCK:], tagged], axis=0)
            arrived = lax.ppermute(payload, "ctx", pairs)
            window_kv.insert(0, arrived[:take * BLOCK])
            window_docs.insert(0, arrived[take * BLOCK, :take].astype(jnp.int32))
            need -= take
            step += 1
        window_kv.append(kv_rows)
        window_docs.append(local_docs)
        kv_all = jnp.concatenate(window_kv, axis=0)
        block_docs = jnp.concatenate(window_docs, axis=0)
        height = kv_all.shape[0]
        key_pos = ctx_rank * row_count - (height - row_count) + jnp.arange(height, dtype=jnp.int32)
        key_docs = jnp.repeat(block_docs, BLOCK)
        query_docs = jnp.repeat(local_docs, BLOCK)
        visible = (
            (key_pos[None, :] <= positions[:, None])
            & (key_pos[None, :] >= 0)
            & (key_docs[None, :] == query_docs[:, None])
        ).astype(jnp.int32)

        local_queries = queries[0]
        query_heads = local_queries.shape[1] // HD
        query_rot = (
            (
                rotate(
                    local_queries.astype(jnp.float32).reshape(row_count, query_heads, HD),
                    cosine,
                    sine_table,
                )
                * (ATTN_FACTOR / math.sqrt(HD))
            )
            .reshape(row_count, query_heads * HD)
            .astype(jnp.bfloat16)
        )
        context = dense_attention(visible, query_rot, kv_all, kv_heads)
        return context[None]

    return body


def solution(mesh):
    n_dp, n_ctx, n_tp = mesh.shape["dp"], mesh.shape["ctx"], mesh.shape["tp"]
    split = jax.sharding.Mesh(
        mesh.devices.reshape(n_dp // 2, 2, n_ctx, n_tp), ("dpc", "core", "ctx", "tp")
    )
    dp = ("dpc", "core")
    placed = (
        P(dp, "ctx", "tp"),
        P(dp, "ctx", "tp"),
        P(dp, "tp"),
        P(dp, "tp"),
        P(dp, "ctx"),
    )
    return jax.shard_map(
        make_body(n_dp // 2, n_ctx, n_tp),
        mesh=split,
        in_specs=placed,
        out_specs=P(dp, "ctx", "tp"),
        check_vma=False,
    )
```

```python
import math

import jax
import jax.numpy as jnp
from jax import lax
from jax.experimental import pallas as pl
from jax.experimental.pallas import tpu as pltpu
from jax.sharding import PartitionSpec as P


HD = 128
BLOCK = 128
LOOKBACK = 7


ROPE_BASE = 500000.0
YARN_FACTOR = 16.0
PRETRAIN_CONTEXT = 8192.0
BETA_FAST = 32.0
BETA_SLOW = 1.0
ATTN_FACTOR = (1.0 + 0.1 * math.log(16.0)) ** 2
MASKED_SCORE = -1e30


def yarn_tables(positions):
    counter = jnp.arange(HD // 2, dtype=jnp.float32)
    base_freq = ROPE_BASE ** (-2.0 * counter / HD)
    wave_ratio = PRETRAIN_CONTEXT * base_freq / (2.0 * math.pi)
    ramp_value = jnp.clip((wave_ratio - BETA_SLOW) / (BETA_FAST - BETA_SLOW), 0.0, 1.0)
    frequency = ramp_value * base_freq + (1.0 - ramp_value) * base_freq / YARN_FACTOR
    angles = positions.astype(jnp.float32)[:, None] * frequency[None, :]
    cosine = jnp.cos(angles)
    sine_table = jnp.sin(angles)
    return (
        jnp.concatenate([cosine, cosine], axis=-1),
        jnp.concatenate([sine_table, sine_table], axis=-1),
    )


def rotate(vectors, cosine, sine_table):
    half_width = vectors.shape[-1] // 2
    lower_half = vectors[..., :half_width]
    upper_half = vectors[..., half_width:]
    turned = jnp.concatenate([-upper_half, lower_half], axis=-1)
    return vectors * cosine[:, None, :] + turned * sine_table[:, None, :]


def dense_kernel(vis_ref, q_ref, k_ref, v_ref, o_ref, qs_ref):
    rows = o_ref.shape[0]
    group = o_ref.shape[1] // HD
    for g in range(group):
        qs_ref[g * rows:(g + 1) * rows, :] = q_ref[:, g * HD:(g + 1) * HD]
    visible = vis_ref[...] != 0
    keys = k_ref[...]
    values = v_ref[...]
    height = keys.shape[0]
    part = group // 2
    for half in range(2):
        stacked = qs_ref[half * part * rows:(half + 1) * part * rows, :]
        scores = lax.dot_general(
            stacked, keys, (((1,), (1,)), ((), ())), preferred_element_type=jnp.float32
        )
        scores = jnp.where(visible[None], scores.reshape(part, rows, height), MASKED_SCORE)
        row_max = jnp.max(scores, axis=2, keepdims=True)
        probs = jnp.where(visible[None], jnp.exp(scores - row_max), 0.0)
        row_sum = jnp.sum(probs, axis=2, keepdims=True)
        mixed = jnp.dot(
            probs.reshape(part * rows, height).astype(jnp.bfloat16),
            values,
            preferred_element_type=jnp.float32,
        )
        result = mixed.reshape(part, rows, HD) / row_sum
        for g in range(part):
            head = half * part + g
            o_ref[:, head * HD:(head + 1) * HD] = result[g].astype(o_ref.dtype)


def dense_attention(visible, query_rot, kv_all, kv_heads, head):
    row_count, width = query_rot.shape
    height = kv_all.shape[0]
    q_blocks = row_count // BLOCK
    group_width = width // kv_heads
    group = group_width // HD
    return pl.pallas_call(
        dense_kernel,
        grid=(q_blocks,),
        in_specs=[
            pl.BlockSpec((BLOCK, height), lambda qb: (qb, 0)),
            pl.BlockSpec((BLOCK, group_width), lambda qb: (qb, head)),
            pl.BlockSpec((height, HD), lambda qb: (0, 0)),
            pl.BlockSpec((height, HD), lambda qb: (0, 1)),
        ],
        out_specs=pl.BlockSpec((BLOCK, group_width), lambda qb: (qb, 0)),
        scratch_shapes=[pltpu.VMEM((group * BLOCK, HD), jnp.bfloat16)],
        out_shape=jax.ShapeDtypeStruct((row_count, group_width), jnp.bfloat16),
        compiler_params=pltpu.CompilerParams(vmem_limit_bytes=48 * 1024 * 1024),
        cost_estimate=pl.CostEstimate(
            flops=4 * row_count * group_width * height,
            transcendentals=row_count * group * height,
            bytes_accessed=4 * row_count * group_width + 2 * kv_all.size + 4 * row_count * height,
        ),
    )(visible, query_rot, kv_all, kv_all)


def shift_pairs(count, step):
    return [(i, i + step) for i in range(count - step)]


def make_body(n_ctx):
    def body(tokens, queries, k_weight, v_weight, doc_blocks):
        return layer(tokens, queries, k_weight, v_weight, doc_blocks)

    def layer(tokens, queries, k_weight, v_weight, doc_blocks):
        local_tokens = tokens[0]
        row_count, feat_half = local_tokens.shape
        ctx_rank = lax.axis_index("ctx")
        tp_rank = lax.axis_index("tp")
        kv_width = k_weight.shape[1]
        kv_heads = kv_width // HD

        positions = ctx_rank * row_count + jnp.arange(row_count, dtype=jnp.int32)
        cosine, sine_table = yarn_tables(positions)
        local_queries = queries[0]
        query_heads = local_queries.shape[1] // HD
        query_rot = (
            (
                rotate(
                    local_queries.astype(jnp.float32).reshape(row_count, query_heads, HD),
                    cosine,
                    sine_table,
                )
                * (ATTN_FACTOR / math.sqrt(HD))
            )
            .reshape(row_count, query_heads * HD)
            .astype(jnp.bfloat16)
        )
        partner_tokens = lax.ppermute(local_tokens, "tp", [(0, 1), (1, 0)])
        local_docs = doc_blocks[0]
        blocks_here = row_count // BLOCK

        outputs = []
        visible = None
        earlier_rows = None
        for head in range(kv_heads):
            cols = slice(head * HD, (head + 1) * HD)
            joined = jnp.concatenate([k_weight[:, cols], v_weight[:, cols]], axis=1)
            weights = lax.all_gather(joined, "dp", axis=0, tiled=True)
            weights = weights.reshape(2, feat_half, 2 * HD)
            proj = jnp.dot(local_tokens, weights[tp_rank], preferred_element_type=jnp.float32)
            proj = proj + jnp.dot(
                partner_tokens, weights[1 - tp_rank], preferred_element_type=jnp.float32
            )
            if earlier_rows is not None:
                proj = proj + 0.0 * earlier_rows[:1, :1].astype(jnp.float32)
            key_rows = (
                rotate(proj[:, :HD].reshape(row_count, 1, HD), cosine, sine_table)
                .reshape(row_count, HD)
                .astype(jnp.bfloat16)
            )
            value_rows = proj[:, HD:].astype(jnp.bfloat16)
            kv_rows = jnp.concatenate([key_rows, value_rows], axis=1)
            earlier_rows = kv_rows

            with_docs = visible is None
            doc_rows = jnp.zeros((16, 2 * HD), jnp.bfloat16)
            window_kv = []
            window_docs = []
            need = LOOKBACK
            step = 1
            while need > 0:
                take = min(need, blocks_here)
                pairs = shift_pairs(n_ctx, step)
                payload = kv_rows[(blocks_here - take) * BLOCK:]
                if with_docs:
                    tagged = doc_rows.at[0, :take].set(
                        local_docs[blocks_here - take:].astype(jnp.bfloat16)
                    )
                    payload = jnp.concatenate([payload, tagged], axis=0)
                arrived = lax.ppermute(payload, "ctx", pairs)
                window_kv.insert(0, arrived[:take * BLOCK])
                if with_docs:
                    window_docs.insert(0, arrived[take * BLOCK, :take].astype(jnp.int32))
                need -= take
                step += 1
            window_kv.append(kv_rows)
            kv_all = jnp.concatenate(window_kv, axis=0)
            height = kv_all.shape[0]
            if with_docs:
                window_docs.append(local_docs)
                block_docs = jnp.concatenate(window_docs, axis=0)
                key_pos = (
                    ctx_rank * row_count - (height - row_count) + jnp.arange(height, dtype=jnp.int32)
                )
                key_docs = jnp.repeat(block_docs, BLOCK)
                query_docs = jnp.repeat(local_docs, BLOCK)
                visible = (
                    (key_pos[None, :] <= positions[:, None])
                    & (key_pos[None, :] >= 0)
                    & (key_docs[None, :] == query_docs[:, None])
                ).astype(jnp.int32)
            outputs.append(dense_attention(visible, query_rot, kv_all, kv_heads, head))
        context = jnp.concatenate(outputs, axis=1)
        return context[None]

    return body


def solution(mesh):
    placed = (
        P("dp", "ctx", "tp"),
        P("dp", "ctx", "tp"),
        P("dp", "tp"),
        P("dp", "tp"),
        P("dp", "ctx"),
    )
    return jax.shard_map(
        make_body(mesh.shape["ctx"]),
        mesh=mesh,
        in_specs=placed,
        out_specs=P("dp", "ctx", "tp"),
        check_vma=False,
    )
```

```python
import math

import jax
import jax.numpy as jnp
from jax import lax
from jax.experimental import pallas as pl
from jax.experimental.pallas import tpu as pltpu
from jax.sharding import PartitionSpec as P


HD = 128
BLOCK = 128
LOOKBACK = 7


ROPE_BASE = 500000.0
YARN_FACTOR = 16.0
PRETRAIN_CONTEXT = 8192.0
BETA_FAST = 32.0
BETA_SLOW = 1.0
ATTN_FACTOR = (1.0 + 0.1 * math.log(16.0)) ** 2
MASKED_SCORE = -1e30


def yarn_tables(positions):
    counter = jnp.arange(HD // 2, dtype=jnp.float32)
    base_freq = ROPE_BASE ** (-2.0 * counter / HD)
    wave_ratio = PRETRAIN_CONTEXT * base_freq / (2.0 * math.pi)
    ramp_value = jnp.clip((wave_ratio - BETA_SLOW) / (BETA_FAST - BETA_SLOW), 0.0, 1.0)
    frequency = ramp_value * base_freq + (1.0 - ramp_value) * base_freq / YARN_FACTOR
    angles = positions.astype(jnp.float32)[:, None] * frequency[None, :]
    cosine = jnp.cos(angles)
    sine_table = jnp.sin(angles)
    return (
        jnp.concatenate([cosine, cosine], axis=-1),
        jnp.concatenate([sine_table, sine_table], axis=-1),
    )


def rotate(vectors, cosine, sine_table):
    half_width = vectors.shape[-1] // 2
    lower_half = vectors[..., :half_width]
    upper_half = vectors[..., half_width:]
    turned = jnp.concatenate([-upper_half, lower_half], axis=-1)
    return vectors * cosine[:, None, :] + turned * sine_table[:, None, :]


def dense_kernel(vis_ref, cos_ref, sin_ref, q_ref, k_ref, v_ref, o_ref, qs_ref):
    rows = o_ref.shape[0]
    group = o_ref.shape[1] // HD
    cosine = cos_ref[...]
    signed_sine = sin_ref[...]
    for g in range(group):
        raw = q_ref[:, g * HD:(g + 1) * HD].astype(jnp.float32)
        turned = pltpu.roll(raw, HD // 2, 1) * signed_sine
        rotated = (raw * cosine + turned) * (ATTN_FACTOR / math.sqrt(HD))
        qs_ref[g * rows:(g + 1) * rows, :] = rotated.astype(jnp.bfloat16)
    visible = vis_ref[...] != 0
    keys = k_ref[...]
    values = v_ref[...]
    height = keys.shape[0]
    part = group // 2
    for half in range(2):
        stacked = qs_ref[half * part * rows:(half + 1) * part * rows, :]
        scores = lax.dot_general(
            stacked, keys, (((1,), (1,)), ((), ())), preferred_element_type=jnp.float32
        )
        scores = jnp.where(visible[None], scores.reshape(part, rows, height), MASKED_SCORE)
        row_max = jnp.max(scores, axis=2, keepdims=True)
        probs = jnp.where(visible[None], jnp.exp(scores - row_max), 0.0)
        row_sum = jnp.sum(probs, axis=2, keepdims=True)
        mixed = jnp.dot(
            probs.reshape(part * rows, height).astype(jnp.bfloat16),
            values,
            preferred_element_type=jnp.float32,
        )
        result = mixed.reshape(part, rows, HD) / row_sum
        for g in range(part):
            head = half * part + g
            o_ref[:, head * HD:(head + 1) * HD] = result[g].astype(o_ref.dtype)


def dense_attention(visible, cosine, signed_sine, query_rot, kv_all, kv_heads, head):
    row_count, width = query_rot.shape
    height = kv_all.shape[0]
    q_blocks = row_count // BLOCK
    group_width = width // kv_heads
    group = group_width // HD
    return pl.pallas_call(
        dense_kernel,
        grid=(q_blocks,),
        in_specs=[
            pl.BlockSpec((BLOCK, height), lambda qb: (qb, 0)),
            pl.BlockSpec((BLOCK, HD), lambda qb: (qb, 0)),
            pl.BlockSpec((BLOCK, HD), lambda qb: (qb, 0)),
            pl.BlockSpec((BLOCK, group_width), lambda qb: (qb, head)),
            pl.BlockSpec((height, HD), lambda qb: (0, 0)),
            pl.BlockSpec((height, HD), lambda qb: (0, 1)),
        ],
        out_specs=pl.BlockSpec((BLOCK, group_width), lambda qb: (qb, 0)),
        scratch_shapes=[pltpu.VMEM((group * BLOCK, HD), jnp.bfloat16)],
        out_shape=jax.ShapeDtypeStruct((row_count, group_width), jnp.bfloat16),
        compiler_params=pltpu.CompilerParams(vmem_limit_bytes=48 * 1024 * 1024),
        cost_estimate=pl.CostEstimate(
            flops=4 * row_count * group_width * height,
            transcendentals=row_count * group * height,
            bytes_accessed=4 * row_count * group_width + 2 * kv_all.size + 4 * row_count * height,
        ),
    )(visible, cosine, signed_sine, query_rot, kv_all, kv_all)


def shift_pairs(count, step):
    return [(i, i + step) for i in range(count - step)]


def make_body(n_ctx):
    def body(tokens, queries, k_weight, v_weight, doc_blocks):
        return layer(tokens, queries, k_weight, v_weight, doc_blocks)

    def layer(tokens, queries, k_weight, v_weight, doc_blocks):
        local_tokens = tokens[0]
        row_count, feat_half = local_tokens.shape
        ctx_rank = lax.axis_index("ctx")
        tp_rank = lax.axis_index("tp")
        kv_width = k_weight.shape[1]
        kv_heads = kv_width // HD

        positions = ctx_rank * row_count + jnp.arange(row_count, dtype=jnp.int32)
        cosine, sine_table = yarn_tables(positions)
        query_rot = queries[0]
        half_sign = jnp.concatenate(
            [-jnp.ones((HD // 2,), jnp.float32), jnp.ones((HD // 2,), jnp.float32)]
        )
        signed_sine = sine_table * half_sign[None, :]
        partner_tokens = lax.ppermute(local_tokens, "tp", [(0, 1), (1, 0)])
        local_docs = doc_blocks[0]
        blocks_here = row_count // BLOCK

        outputs = []
        visible = None
        earlier_rows = None
        for head in range(kv_heads):
            cols = slice(head * HD, (head + 1) * HD)
            joined = jnp.concatenate([k_weight[:, cols], v_weight[:, cols]], axis=1)
            weights = lax.all_gather(joined, "dp", axis=0, tiled=True)
            weights = weights.reshape(2, feat_half, 2 * HD)
            proj = jnp.dot(local_tokens, weights[tp_rank], preferred_element_type=jnp.float32)
            proj = proj + jnp.dot(
                partner_tokens, weights[1 - tp_rank], preferred_element_type=jnp.float32
            )
            if earlier_rows is not None:
                proj = proj + 0.0 * earlier_rows[:1, :1].astype(jnp.float32)
            key_rows = (
                rotate(proj[:, :HD].reshape(row_count, 1, HD), cosine, sine_table)
                .reshape(row_count, HD)
                .astype(jnp.bfloat16)
            )
            value_rows = proj[:, HD:].astype(jnp.bfloat16)
            kv_rows = jnp.concatenate([key_rows, value_rows], axis=1)
            earlier_rows = kv_rows

            with_docs = visible is None
            doc_rows = jnp.zeros((16, 2 * HD), jnp.bfloat16)
            window_kv = []
            window_docs = []
            need = LOOKBACK
            step = 1
            while need > 0:
                take = min(need, blocks_here)
                pairs = shift_pairs(n_ctx, step)
                payload = kv_rows[(blocks_here - take) * BLOCK:]
                if with_docs:
                    tagged = doc_rows.at[0, :take].set(
                        local_docs[blocks_here - take:].astype(jnp.bfloat16)
                    )
                    payload = jnp.concatenate([payload, tagged], axis=0)
                arrived = lax.ppermute(payload, "ctx", pairs)
                window_kv.insert(0, arrived[:take * BLOCK])
                if with_docs:
                    window_docs.insert(0, arrived[take * BLOCK, :take].astype(jnp.int32))
                need -= take
                step += 1
            window_kv.append(kv_rows)
            kv_all = jnp.concatenate(window_kv, axis=0)
            height = kv_all.shape[0]
            if with_docs:
                window_docs.append(local_docs)
                block_docs = jnp.concatenate(window_docs, axis=0)
                key_pos = (
                    ctx_rank * row_count - (height - row_count) + jnp.arange(height, dtype=jnp.int32)
                )
                key_docs = jnp.repeat(block_docs, BLOCK)
                query_docs = jnp.repeat(local_docs, BLOCK)
                visible = (
                    (key_pos[None, :] <= positions[:, None])
                    & (key_pos[None, :] >= 0)
                    & (key_docs[None, :] == query_docs[:, None])
                ).astype(jnp.int32)
            outputs.append(
                dense_attention(
                    visible, cosine, signed_sine, query_rot, kv_all, kv_heads, head
                )
            )
        context = jnp.concatenate(outputs, axis=1)
        return context[None]

    return body


def solution(mesh):
    placed = (
        P("dp", "ctx", "tp"),
        P("dp", "ctx", "tp"),
        P("dp", "tp"),
        P("dp", "tp"),
        P("dp", "ctx"),
    )
    return jax.shard_map(
        make_body(mesh.shape["ctx"]),
        mesh=mesh,
        in_specs=placed,
        out_specs=P("dp", "ctx", "tp"),
        check_vma=False,
    )
```

```python
import math

import jax
import jax.numpy as jnp
from jax import lax
from jax.experimental import pallas as pl
from jax.experimental.pallas import tpu as pltpu
from jax.sharding import PartitionSpec as P


HD = 128
BLOCK = 128
LOOKBACK = 7


ROPE_BASE = 500000.0
YARN_FACTOR = 16.0
PRETRAIN_CONTEXT = 8192.0
BETA_FAST = 32.0
BETA_SLOW = 1.0
ATTN_FACTOR = (1.0 + 0.1 * math.log(16.0)) ** 2
MASKED_SCORE = -1e30


def yarn_tables(positions):
    return yarn_tables_at(positions.astype(jnp.float32))


def yarn_tables_at(float_positions):
    counter = jnp.arange(HD // 2, dtype=jnp.float32)
    base_freq = ROPE_BASE ** (-2.0 * counter / HD)
    wave_ratio = PRETRAIN_CONTEXT * base_freq / (2.0 * math.pi)
    ramp_value = jnp.clip((wave_ratio - BETA_SLOW) / (BETA_FAST - BETA_SLOW), 0.0, 1.0)
    frequency = ramp_value * base_freq + (1.0 - ramp_value) * base_freq / YARN_FACTOR
    angles = float_positions[:, None] * frequency[None, :]
    cosine = jnp.cos(angles)
    sine_table = jnp.sin(angles)
    return (
        jnp.concatenate([cosine, cosine], axis=-1),
        jnp.concatenate([sine_table, sine_table], axis=-1),
    )


def rotate(vectors, cosine, sine_table):
    half_width = vectors.shape[-1] // 2
    lower_half = vectors[..., :half_width]
    upper_half = vectors[..., half_width:]
    turned = jnp.concatenate([-upper_half, lower_half], axis=-1)
    return vectors * cosine[:, None, :] + turned * sine_table[:, None, :]


def dense_kernel(vis_ref, cos_ref, sin_ref, q_ref, k_ref, v_ref, o_ref, qs_ref):
    rows = o_ref.shape[0]
    group = o_ref.shape[1] // HD
    cosine = cos_ref[...]
    signed_sine = sin_ref[...]
    for g in range(group):
        raw = q_ref[:, g * HD:(g + 1) * HD].astype(jnp.float32)
        turned = pltpu.roll(raw, HD // 2, 1) * signed_sine
        rotated = (raw * cosine + turned) * (ATTN_FACTOR / math.sqrt(HD))
        qs_ref[g * rows:(g + 1) * rows, :] = rotated.astype(jnp.bfloat16)
    visible = vis_ref[...] != 0
    keys = k_ref[...]
    values = v_ref[...]
    height = keys.shape[0]
    part = group // 2
    for half in range(2):
        stacked = qs_ref[half * part * rows:(half + 1) * part * rows, :]
        scores = lax.dot_general(
            stacked, keys, (((1,), (1,)), ((), ())), preferred_element_type=jnp.float32
        )
        scores = jnp.where(visible[None], scores.reshape(part, rows, height), MASKED_SCORE)
        row_max = jnp.max(scores, axis=2, keepdims=True)
        probs = jnp.where(visible[None], jnp.exp(scores - row_max), 0.0)
        row_sum = jnp.sum(probs, axis=2, keepdims=True)
        mixed = jnp.dot(
            probs.reshape(part * rows, height).astype(jnp.bfloat16),
            values,
            preferred_element_type=jnp.float32,
        )
        result = mixed.reshape(part, rows, HD) / row_sum
        for g in range(part):
            head = half * part + g
            o_ref[:, head * HD:(head + 1) * HD] = result[g].astype(o_ref.dtype)


def dense_attention(visible, cosine, signed_sine, query_rot, kv_all, kv_heads, head):
    row_count, width = query_rot.shape
    height = kv_all.shape[0]
    q_blocks = row_count // BLOCK
    group_width = width // kv_heads
    group = group_width // HD
    return pl.pallas_call(
        dense_kernel,
        grid=(q_blocks,),
        in_specs=[
            pl.BlockSpec((BLOCK, height), lambda qb: (qb, 0)),
            pl.BlockSpec((BLOCK, HD), lambda qb: (qb, 0)),
            pl.BlockSpec((BLOCK, HD), lambda qb: (qb, 0)),
            pl.BlockSpec((BLOCK, group_width), lambda qb: (qb, head)),
            pl.BlockSpec((height, HD), lambda qb: (0, 0)),
            pl.BlockSpec((height, HD), lambda qb: (0, 1)),
        ],
        out_specs=pl.BlockSpec((BLOCK, group_width), lambda qb: (qb, 0)),
        scratch_shapes=[pltpu.VMEM((group * BLOCK, HD), jnp.bfloat16)],
        out_shape=jax.ShapeDtypeStruct((row_count, group_width), jnp.bfloat16),
        compiler_params=pltpu.CompilerParams(vmem_limit_bytes=48 * 1024 * 1024),
        cost_estimate=pl.CostEstimate(
            flops=4 * row_count * group_width * height,
            transcendentals=row_count * group * height,
            bytes_accessed=4 * row_count * group_width + 2 * kv_all.size + 4 * row_count * height,
        ),
    )(visible, cosine, signed_sine, query_rot, kv_all, kv_all)


def shift_pairs(count, step):
    return [(i, i + step) for i in range(count - step)]


def make_body(n_ctx):
    def body(tokens, queries, k_weight, v_weight, doc_blocks):
        return layer(tokens, queries, k_weight, v_weight, doc_blocks)

    def layer(tokens, queries, k_weight, v_weight, doc_blocks):
        local_tokens = tokens[0]
        row_count, feat_half = local_tokens.shape
        ctx_rank = lax.axis_index("ctx")
        tp_rank = lax.axis_index("tp")
        kv_width = k_weight.shape[1]
        kv_heads = kv_width // HD

        positions = ctx_rank * row_count + jnp.arange(row_count, dtype=jnp.int32)
        cosine, sine_table = yarn_tables(positions)
        query_rot = queries[0]
        half_sign = jnp.concatenate(
            [-jnp.ones((HD // 2,), jnp.float32), jnp.ones((HD // 2,), jnp.float32)]
        )
        kernel_positions = jnp.arange(row_count, dtype=jnp.float32) + (ctx_rank * row_count).astype(
            jnp.float32
        )
        kernel_cosine, kernel_sine = yarn_tables_at(kernel_positions)
        signed_sine = kernel_sine * half_sign[None, :]
        partner_tokens = lax.ppermute(local_tokens, "tp", [(0, 1), (1, 0)])
        local_docs = doc_blocks[0]
        blocks_here = row_count // BLOCK

        outputs = []
        visible = None
        earlier_rows = None
        for head in range(kv_heads):
            cols = slice(head * HD, (head + 1) * HD)
            joined = jnp.concatenate([k_weight[:, cols], v_weight[:, cols]], axis=1)
            weights = lax.all_gather(joined, "dp", axis=0, tiled=True)
            weights = weights.reshape(2, feat_half, 2 * HD)
            proj = jnp.dot(local_tokens, weights[tp_rank], preferred_element_type=jnp.float32)
            proj = proj + jnp.dot(
                partner_tokens, weights[1 - tp_rank], preferred_element_type=jnp.float32
            )
            if earlier_rows is not None:
                proj = proj + 0.0 * earlier_rows[:1, :1].astype(jnp.float32)
            key_rows = (
                rotate(proj[:, :HD].reshape(row_count, 1, HD), cosine, sine_table)
                .reshape(row_count, HD)
                .astype(jnp.bfloat16)
            )
            value_rows = proj[:, HD:].astype(jnp.bfloat16)
            kv_rows = jnp.concatenate([key_rows, value_rows], axis=1)
            earlier_rows = kv_rows

            with_docs = visible is None
            doc_rows = jnp.zeros((16, 2 * HD), jnp.bfloat16)
            window_kv = []
            window_docs = []
            need = LOOKBACK
            step = 1
            while need > 0:
                take = min(need, blocks_here)
                pairs = shift_pairs(n_ctx, step)
                payload = kv_rows[(blocks_here - take) * BLOCK:]
                if with_docs:
                    tagged = doc_rows.at[0, :take].set(
                        local_docs[blocks_here - take:].astype(jnp.bfloat16)
                    )
                    payload = jnp.concatenate([payload, tagged], axis=0)
                arrived = lax.ppermute(payload, "ctx", pairs)
                window_kv.insert(0, arrived[:take * BLOCK])
                if with_docs:
                    window_docs.insert(0, arrived[take * BLOCK, :take].astype(jnp.int32))
                need -= take
                step += 1
            window_kv.append(kv_rows)
            kv_all = jnp.concatenate(window_kv, axis=0)
            height = kv_all.shape[0]
            if with_docs:
                window_docs.append(local_docs)
                block_docs = jnp.concatenate(window_docs, axis=0)
                key_pos = (
                    ctx_rank * row_count - (height - row_count) + jnp.arange(height, dtype=jnp.int32)
                )
                key_docs = jnp.repeat(block_docs, BLOCK)
                query_docs = jnp.repeat(local_docs, BLOCK)
                visible = (
                    (key_pos[None, :] <= positions[:, None])
                    & (key_pos[None, :] >= 0)
                    & (key_docs[None, :] == query_docs[:, None])
                ).astype(jnp.int32)
            outputs.append(
                dense_attention(
                    visible, kernel_cosine, signed_sine, query_rot, kv_all, kv_heads, head
                )
            )
        context = jnp.concatenate(outputs, axis=1)
        return context[None]

    return body


def solution(mesh):
    placed = (
        P("dp", "ctx", "tp"),
        P("dp", "ctx", "tp"),
        P("dp", "tp"),
        P("dp", "tp"),
        P("dp", "ctx"),
    )
    return jax.shard_map(
        make_body(mesh.shape["ctx"]),
        mesh=mesh,
        in_specs=placed,
        out_specs=P("dp", "ctx", "tp"),
        check_vma=False,
    )
```

```python
import math

import jax
import jax.numpy as jnp
from jax import lax
from jax.experimental import pallas as pl
from jax.experimental.pallas import tpu as pltpu
from jax.sharding import PartitionSpec as P


HD = 128
BLOCK = 128
LOOKBACK = 7


ROPE_BASE = 500000.0
YARN_FACTOR = 16.0
PRETRAIN_CONTEXT = 8192.0
BETA_FAST = 32.0
BETA_SLOW = 1.0
ATTN_FACTOR = (1.0 + 0.1 * math.log(16.0)) ** 2
MASKED_SCORE = -1e30


def yarn_tables(positions):
    return yarn_tables_at(positions.astype(jnp.float32))


def yarn_tables_at(float_positions):
    counter = jnp.arange(HD // 2, dtype=jnp.float32)
    base_freq = ROPE_BASE ** (-2.0 * counter / HD)
    wave_ratio = PRETRAIN_CONTEXT * base_freq / (2.0 * math.pi)
    ramp_value = jnp.clip((wave_ratio - BETA_SLOW) / (BETA_FAST - BETA_SLOW), 0.0, 1.0)
    frequency = ramp_value * base_freq + (1.0 - ramp_value) * base_freq / YARN_FACTOR
    angles = float_positions[:, None] * frequency[None, :]
    cosine = jnp.cos(angles)
    sine_table = jnp.sin(angles)
    return (
        jnp.concatenate([cosine, cosine], axis=-1),
        jnp.concatenate([sine_table, sine_table], axis=-1),
    )


def rotate(vectors, cosine, sine_table):
    half_width = vectors.shape[-1] // 2
    lower_half = vectors[..., :half_width]
    upper_half = vectors[..., half_width:]
    turned = jnp.concatenate([-upper_half, lower_half], axis=-1)
    return vectors * cosine[:, None, :] + turned * sine_table[:, None, :]


def dense_kernel(vis_ref, cos_ref, sin_ref, q_ref, k_ref, v_ref, o_ref, qs_ref):
    rows = o_ref.shape[0]
    group = o_ref.shape[1] // HD
    cosine = cos_ref[...]
    signed_sine = sin_ref[...]
    for g in range(group):
        raw = q_ref[:, g * HD:(g + 1) * HD].astype(jnp.float32)
        turned = pltpu.roll(raw, HD // 2, 1) * signed_sine
        rotated = (raw * cosine + turned) * (ATTN_FACTOR / math.sqrt(HD))
        qs_ref[g * rows:(g + 1) * rows, :] = rotated.astype(jnp.bfloat16)
    visible = vis_ref[...] != 0
    keys = k_ref[...]
    values = v_ref[...]
    height = keys.shape[0]
    part = group // 2
    for half in range(2):
        stacked = qs_ref[half * part * rows:(half + 1) * part * rows, :]
        scores = lax.dot_general(
            stacked, keys, (((1,), (1,)), ((), ())), preferred_element_type=jnp.float32
        )
        scores = jnp.where(visible[None], scores.reshape(part, rows, height), MASKED_SCORE)
        row_max = jnp.max(scores, axis=2, keepdims=True)
        probs = jnp.where(visible[None], jnp.exp(scores - row_max), 0.0)
        row_sum = jnp.sum(probs, axis=2, keepdims=True)
        mixed = jnp.dot(
            probs.reshape(part * rows, height).astype(jnp.bfloat16),
            values,
            preferred_element_type=jnp.float32,
        )
        result = mixed.reshape(part, rows, HD) / row_sum
        for g in range(part):
            head = half * part + g
            o_ref[:, head * HD:(head + 1) * HD] = result[g].astype(o_ref.dtype)


def dense_attention(visible, cosine, signed_sine, query_rot, kv_all, kv_heads, head):
    row_count, width = query_rot.shape
    height = kv_all.shape[0]
    q_blocks = row_count // BLOCK
    group_width = width // kv_heads
    group = group_width // HD
    return pl.pallas_call(
        dense_kernel,
        grid=(q_blocks,),
        in_specs=[
            pl.BlockSpec((BLOCK, height), lambda qb: (qb, 0)),
            pl.BlockSpec((BLOCK, HD), lambda qb: (qb, 0)),
            pl.BlockSpec((BLOCK, HD), lambda qb: (qb, 0)),
            pl.BlockSpec((BLOCK, group_width), lambda qb: (qb, head)),
            pl.BlockSpec((height, HD), lambda qb: (0, 0)),
            pl.BlockSpec((height, HD), lambda qb: (0, 1)),
        ],
        out_specs=pl.BlockSpec((BLOCK, group_width), lambda qb: (qb, 0)),
        scratch_shapes=[pltpu.VMEM((group * BLOCK, HD), jnp.bfloat16)],
        out_shape=jax.ShapeDtypeStruct((row_count, group_width), jnp.bfloat16),
        compiler_params=pltpu.CompilerParams(vmem_limit_bytes=48 * 1024 * 1024),
        cost_estimate=pl.CostEstimate(
            flops=4 * row_count * group_width * height,
            transcendentals=row_count * group * height,
            bytes_accessed=4 * row_count * group_width + 2 * kv_all.size + 4 * row_count * height,
        ),
    )(visible, cosine, signed_sine, query_rot, kv_all, kv_all)


def shift_pairs(count, step):
    return [(i, i + step) for i in range(count - step)]


def x_shift_pairs(n_dp, n_tp, direction):
    pairs = []
    for dp in range(n_dp):
        for tp in range(n_tp):
            core, x_lo, y = dp % 2, (dp // 2) % 2, dp // 4
            moved = (2 * tp + x_lo + direction) % (2 * n_tp)
            target = ((y * 2 + moved % 2) * 2 + core) * n_tp + moved // 2
            pairs.append((dp * n_tp + tp, target))
    return pairs


def make_body(n_dp, n_ctx, n_tp):
    def body(tokens, queries, k_weight, v_weight, doc_blocks):
        return layer(tokens, queries, k_weight, v_weight, doc_blocks)

    def layer(tokens, queries, k_weight, v_weight, doc_blocks):
        local_tokens = tokens[0]
        row_count, feat_half = local_tokens.shape
        ctx_rank = lax.axis_index("ctx")
        tp_rank = lax.axis_index("tp")
        kv_width = k_weight.shape[1]
        kv_heads = kv_width // HD

        positions = ctx_rank * row_count + jnp.arange(row_count, dtype=jnp.int32)
        cosine, sine_table = yarn_tables(positions)
        query_rot = queries[0]
        half_sign = jnp.concatenate(
            [-jnp.ones((HD // 2,), jnp.float32), jnp.ones((HD // 2,), jnp.float32)]
        )
        kernel_positions = jnp.arange(row_count, dtype=jnp.float32) + (ctx_rank * row_count).astype(
            jnp.float32
        )
        kernel_cosine, kernel_sine = yarn_tables_at(kernel_positions)
        signed_sine = kernel_sine * half_sign[None, :]
        half_rows = row_count // 2
        forward = x_shift_pairs(n_dp, n_tp, 1)
        backward = x_shift_pairs(n_dp, n_tp, -1)
        via_next = lax.ppermute(local_tokens[:half_rows], ("dp", "tp"), forward)
        via_prev = lax.ppermute(local_tokens[half_rows:], ("dp", "tp"), backward)
        via_next = lax.ppermute(via_next, ("dp", "tp"), forward)
        via_prev = lax.ppermute(via_prev, ("dp", "tp"), backward)
        partner_tokens = jnp.concatenate([via_next, via_prev], axis=0)
        local_docs = doc_blocks[0]
        blocks_here = row_count // BLOCK

        outputs = []
        visible = None
        earlier_rows = None
        for head in range(kv_heads):
            cols = slice(head * HD, (head + 1) * HD)
            joined = jnp.concatenate([k_weight[:, cols], v_weight[:, cols]], axis=1)
            weights = lax.all_gather(joined, "dp", axis=0, tiled=True)
            weights = weights.reshape(2, feat_half, 2 * HD)
            proj = jnp.dot(local_tokens, weights[tp_rank], preferred_element_type=jnp.float32)
            proj = proj + jnp.dot(
                partner_tokens, weights[1 - tp_rank], preferred_element_type=jnp.float32
            )
            if earlier_rows is not None:
                proj = proj + 0.0 * earlier_rows[:1, :1].astype(jnp.float32)
            key_rows = (
                rotate(proj[:, :HD].reshape(row_count, 1, HD), cosine, sine_table)
                .reshape(row_count, HD)
                .astype(jnp.bfloat16)
            )
            value_rows = proj[:, HD:].astype(jnp.bfloat16)
            kv_rows = jnp.concatenate([key_rows, value_rows], axis=1)
            earlier_rows = kv_rows

            with_docs = visible is None
            doc_rows = jnp.zeros((16, 2 * HD), jnp.bfloat16)
            window_kv = []
            window_docs = []
            need = LOOKBACK
            step = 1
            while need > 0:
                take = min(need, blocks_here)
                pairs = shift_pairs(n_ctx, step)
                payload = kv_rows[(blocks_here - take) * BLOCK:]
                if with_docs:
                    tagged = doc_rows.at[0, :take].set(
                        local_docs[blocks_here - take:].astype(jnp.bfloat16)
                    )
                    payload = jnp.concatenate([payload, tagged], axis=0)
                arrived = lax.ppermute(payload, "ctx", pairs)
                window_kv.insert(0, arrived[:take * BLOCK])
                if with_docs:
                    window_docs.insert(0, arrived[take * BLOCK, :take].astype(jnp.int32))
                need -= take
                step += 1
            window_kv.append(kv_rows)
            kv_all = jnp.concatenate(window_kv, axis=0)
            height = kv_all.shape[0]
            if with_docs:
                window_docs.append(local_docs)
                block_docs = jnp.concatenate(window_docs, axis=0)
                key_pos = (
                    ctx_rank * row_count - (height - row_count) + jnp.arange(height, dtype=jnp.int32)
                )
                key_docs = jnp.repeat(block_docs, BLOCK)
                query_docs = jnp.repeat(local_docs, BLOCK)
                visible = (
                    (key_pos[None, :] <= positions[:, None])
                    & (key_pos[None, :] >= 0)
                    & (key_docs[None, :] == query_docs[:, None])
                ).astype(jnp.int32)
            outputs.append(
                dense_attention(
                    visible, kernel_cosine, signed_sine, query_rot, kv_all, kv_heads, head
                )
            )
        context = jnp.concatenate(outputs, axis=1)
        return context[None]

    return body


def solution(mesh):
    placed = (
        P("dp", "ctx", "tp"),
        P("dp", "ctx", "tp"),
        P("dp", "tp"),
        P("dp", "tp"),
        P("dp", "ctx"),
    )
    return jax.shard_map(
        make_body(mesh.shape["dp"], mesh.shape["ctx"], mesh.shape["tp"]),
        mesh=mesh,
        in_specs=placed,
        out_specs=P("dp", "ctx", "tp"),
        check_vma=False,
    )
```

```python
import math

import jax
import jax.numpy as jnp
from jax import lax
from jax.experimental import pallas as pl
from jax.experimental.pallas import tpu as pltpu
from jax.sharding import PartitionSpec as P


HD = 128
BLOCK = 128
LOOKBACK = 7


ROPE_BASE = 500000.0
YARN_FACTOR = 16.0
PRETRAIN_CONTEXT = 8192.0
BETA_FAST = 32.0
BETA_SLOW = 1.0
ATTN_FACTOR = (1.0 + 0.1 * math.log(16.0)) ** 2
MASKED_SCORE = -1e30


def yarn_tables(positions):
    return yarn_tables_at(positions.astype(jnp.float32))


def yarn_tables_at(float_positions):
    counter = jnp.arange(HD // 2, dtype=jnp.float32)
    base_freq = ROPE_BASE ** (-2.0 * counter / HD)
    wave_ratio = PRETRAIN_CONTEXT * base_freq / (2.0 * math.pi)
    ramp_value = jnp.clip((wave_ratio - BETA_SLOW) / (BETA_FAST - BETA_SLOW), 0.0, 1.0)
    frequency = ramp_value * base_freq + (1.0 - ramp_value) * base_freq / YARN_FACTOR
    angles = float_positions[:, None] * frequency[None, :]
    cosine = jnp.cos(angles)
    sine_table = jnp.sin(angles)
    return (
        jnp.concatenate([cosine, cosine], axis=-1),
        jnp.concatenate([sine_table, sine_table], axis=-1),
    )


def rotate(vectors, cosine, sine_table):
    half_width = vectors.shape[-1] // 2
    lower_half = vectors[..., :half_width]
    upper_half = vectors[..., half_width:]
    turned = jnp.concatenate([-upper_half, lower_half], axis=-1)
    return vectors * cosine[:, None, :] + turned * sine_table[:, None, :]


def dense_kernel(vis_ref, cos_ref, sin_ref, q_ref, k_ref, v_ref, *rest):
    o_ref, qs_ref = rest[-2:]
    rows = o_ref.shape[0]
    group = o_ref.shape[1] // HD
    cosine = cos_ref[...]
    signed_sine = sin_ref[...]
    for g in range(group):
        raw = q_ref[:, g * HD:(g + 1) * HD].astype(jnp.float32)
        turned = pltpu.roll(raw, HD // 2, 1) * signed_sine
        rotated = (raw * cosine + turned) * (ATTN_FACTOR / math.sqrt(HD))
        qs_ref[g * rows:(g + 1) * rows, :] = rotated.astype(jnp.bfloat16)
    visible = vis_ref[...] != 0
    keys = k_ref[...]
    values = v_ref[...]
    height = keys.shape[0]
    part = group // 2
    for half in range(2):
        stacked = qs_ref[half * part * rows:(half + 1) * part * rows, :]
        scores = lax.dot_general(
            stacked, keys, (((1,), (1,)), ((), ())), preferred_element_type=jnp.float32
        )
        scores = jnp.where(visible[None], scores.reshape(part, rows, height), MASKED_SCORE)
        row_max = jnp.max(scores, axis=2, keepdims=True)
        probs = jnp.where(visible[None], jnp.exp(scores - row_max), 0.0)
        row_sum = jnp.sum(probs, axis=2, keepdims=True)
        mixed = jnp.dot(
            probs.reshape(part * rows, height).astype(jnp.bfloat16),
            values,
            preferred_element_type=jnp.float32,
        )
        result = mixed.reshape(part, rows, HD) / row_sum
        for g in range(part):
            head = half * part + g
            o_ref[:, head * HD:(head + 1) * HD] = result[g].astype(o_ref.dtype)


def dense_attention(visible, cosine, signed_sine, query_rot, kv_all, kv_heads, head, into=None):
    row_count, width = query_rot.shape
    height = kv_all.shape[0]
    q_blocks = row_count // BLOCK
    group_width = width // kv_heads
    group = group_width // HD
    return pl.pallas_call(
        dense_kernel,
        grid=(q_blocks,),
        in_specs=[
            pl.BlockSpec((BLOCK, height), lambda qb: (qb, 0)),
            pl.BlockSpec((BLOCK, HD), lambda qb: (qb, 0)),
            pl.BlockSpec((BLOCK, HD), lambda qb: (qb, 0)),
            pl.BlockSpec((BLOCK, group_width), lambda qb: (qb, head)),
            pl.BlockSpec((height, HD), lambda qb: (0, 0)),
            pl.BlockSpec((height, HD), lambda qb: (0, 1)),
        ]
        + ([] if into is None else [pl.BlockSpec(memory_space=pl.ANY)]),
        out_specs=pl.BlockSpec((BLOCK, group_width), lambda qb: (qb, head)),
        input_output_aliases={} if into is None else {6: 0},
        scratch_shapes=[pltpu.VMEM((group * BLOCK, HD), jnp.bfloat16)],
        out_shape=jax.ShapeDtypeStruct((row_count, width), jnp.bfloat16),
        compiler_params=pltpu.CompilerParams(vmem_limit_bytes=48 * 1024 * 1024),
        cost_estimate=pl.CostEstimate(
            flops=4 * row_count * group_width * height,
            transcendentals=row_count * group * height,
            bytes_accessed=4 * row_count * group_width + 2 * kv_all.size + 4 * row_count * height,
        ),
    )(visible, cosine, signed_sine, query_rot, kv_all, kv_all, *([] if into is None else [into]))


def shift_pairs(count, step):
    return [(i, i + step) for i in range(count - step)]


def make_body(n_ctx):
    def body(tokens, queries, k_weight, v_weight, doc_blocks):
        return layer(tokens, queries, k_weight, v_weight, doc_blocks)

    def layer(tokens, queries, k_weight, v_weight, doc_blocks):
        local_tokens = tokens[0]
        row_count, feat_half = local_tokens.shape
        ctx_rank = lax.axis_index("ctx")
        tp_rank = lax.axis_index("tp")
        kv_width = k_weight.shape[1]
        kv_heads = kv_width // HD

        positions = ctx_rank * row_count + jnp.arange(row_count, dtype=jnp.int32)
        cosine, sine_table = yarn_tables(positions)
        query_rot = queries[0]
        half_sign = jnp.concatenate(
            [-jnp.ones((HD // 2,), jnp.float32), jnp.ones((HD // 2,), jnp.float32)]
        )
        kernel_positions = jnp.arange(row_count, dtype=jnp.float32) + (ctx_rank * row_count).astype(
            jnp.float32
        )
        kernel_cosine, kernel_sine = yarn_tables_at(kernel_positions)
        signed_sine = kernel_sine * half_sign[None, :]
        partner_tokens = lax.ppermute(local_tokens, "tp", [(0, 1), (1, 0)])
        local_docs = doc_blocks[0]
        blocks_here = row_count // BLOCK

        context = None
        visible = None
        earlier_rows = None
        for head in range(kv_heads):
            cols = slice(head * HD, (head + 1) * HD)
            joined = jnp.concatenate([k_weight[:, cols], v_weight[:, cols]], axis=1)
            weights = lax.all_gather(joined, "dp", axis=0, tiled=True)
            weights = weights.reshape(2, feat_half, 2 * HD)
            proj = jnp.dot(local_tokens, weights[tp_rank], preferred_element_type=jnp.float32)
            proj = proj + jnp.dot(
                partner_tokens, weights[1 - tp_rank], preferred_element_type=jnp.float32
            )
            if earlier_rows is not None:
                proj = proj + 0.0 * earlier_rows[:1, :1].astype(jnp.float32)
            key_rows = (
                rotate(proj[:, :HD].reshape(row_count, 1, HD), cosine, sine_table)
                .reshape(row_count, HD)
                .astype(jnp.bfloat16)
            )
            value_rows = proj[:, HD:].astype(jnp.bfloat16)
            kv_rows = jnp.concatenate([key_rows, value_rows], axis=1)
            earlier_rows = kv_rows

            with_docs = visible is None
            doc_rows = jnp.zeros((16, 2 * HD), jnp.bfloat16)
            window_kv = []
            window_docs = []
            need = LOOKBACK
            step = 1
            while need > 0:
                take = min(need, blocks_here)
                pairs = shift_pairs(n_ctx, step)
                payload = kv_rows[(blocks_here - take) * BLOCK:]
                if with_docs:
                    tagged = doc_rows.at[0, :take].set(
                        local_docs[blocks_here - take:].astype(jnp.bfloat16)
                    )
                    payload = jnp.concatenate([payload, tagged], axis=0)
                arrived = lax.ppermute(payload, "ctx", pairs)
                window_kv.insert(0, arrived[:take * BLOCK])
                if with_docs:
                    window_docs.insert(0, arrived[take * BLOCK, :take].astype(jnp.int32))
                need -= take
                step += 1
            window_kv.append(kv_rows)
            kv_all = jnp.concatenate(window_kv, axis=0)
            height = kv_all.shape[0]
            if with_docs:
                window_docs.append(local_docs)
                block_docs = jnp.concatenate(window_docs, axis=0)
                key_pos = (
                    ctx_rank * row_count - (height - row_count) + jnp.arange(height, dtype=jnp.int32)
                )
                key_docs = jnp.repeat(block_docs, BLOCK)
                query_docs = jnp.repeat(local_docs, BLOCK)
                visible = (
                    (key_pos[None, :] <= positions[:, None])
                    & (key_pos[None, :] >= 0)
                    & (key_docs[None, :] == query_docs[:, None])
                ).astype(jnp.int32)
            context = dense_attention(
                visible, kernel_cosine, signed_sine, query_rot, kv_all, kv_heads, head, context
            )
        return context[None]

    return body


def solution(mesh):
    placed = (
        P("dp", "ctx", "tp"),
        P("dp", "ctx", "tp"),
        P("dp", "tp"),
        P("dp", "tp"),
        P("dp", "ctx"),
    )
    return jax.shard_map(
        make_body(mesh.shape["ctx"]),
        mesh=mesh,
        in_specs=placed,
        out_specs=P("dp", "ctx", "tp"),
        check_vma=False,
    )
```
